128 devices in a mesh: pair: 32 (over z, y, core), integral: 4 (over x).
Axes of the slice: x: 4, y: 4, z: 4, core: 2. Of those that a mesh axis runs over, the one named last changes fastest.
Arguments:
- occ_irrep: int32 [240], replicated, may hold values from 0 to 7
- amplitudes: bfloat16 [1920, 16384], P('pair', 'integral'), may hold values from -6 to 6
- ladder_ints: bfloat16 [16384, 16384], P('integral', 'pair'), may hold values from -0.046875 to 0.046875
- cycle_ints: bfloat16 [240, 128, 30720], P(None, 'integral', 'pair'), may hold values from -0.03125 to 0.03125
Outputs:
- residual: float32 [8, 240, 16384], P('integral', None, 'pair')
The draws below stay inside these ranges and needn't reach their ends.
Inputs may be any that keep to these rules, and one draw needn't show every extreme that they name: `occ_irrep`: irrep labels of D2h, below 8.
All inputs are finite; a program needn't handle non-finite values.
Results may differ from the reference program's by a relative error of at most 0.0003.
Values may be sent and summed in bfloat16 or wider, within the bound.
No kernel may reach another device: no remote copies, remote signals or barrier semaphores. Data moves between devices by JAX's collectives and lax.ppermute only.
A program may use at most 192 MiB of HBM per device.

```python
import math
import jax
import jax.numpy as jnp
import numpy as np
from jax import lax

OCC = 240
VIRT = 128
IWIN = 8
OPAIRS = 1920


def touch_ends(drawn, own_key, least, largest):
    index_at = [jax.random.randint(jax.random.fold_in(own_key, axis), (), 0, length) for axis, length in enumerate(drawn.shape)]
    main_axis = drawn.shape.index(max(drawn.shape))
    beside = index_at[:main_axis] + [(index_at[main_axis] + 1) % drawn.shape[main_axis]] + index_at[main_axis + 1:]
    return drawn.at[tuple(index_at)].set(least).at[tuple(beside)].set(largest)


def steps_of(key, extent, pieces, least, high):
    gain = 1.0
    for position, parts in pieces:
        draws = jax.random.uniform(jax.random.fold_in(jax.random.fold_in(key, 6), position), (parts,), jnp.float32, least / len(pieces), high / len(pieces))
        gain = gain * jnp.repeat(jnp.exp(draws), extent[position] // parts).reshape((-1,) + (1,) * (len(extent) - 1 - position))
    return gain


def rank_bounds(amount, lean):
    loads = [(1 << 20) // math.isqrt(standing ** lean) + 1 for standing in range(1, amount + 1)]
    spread = 1 + sum(loads) // (1 << 30)
    return np.cumsum(np.array([max(1, weight // spread) for weight in loads]))


def ranked_ids(rng, extent, count, lean):
    listing = rank_bounds(count, lean)
    ticket = jax.random.randint(jax.random.fold_in(rng, 1), extent, 0, int(listing[count - 1]))
    standing = jnp.searchsorted(jnp.asarray(listing, jnp.int32), ticket, side="right")
    return jax.random.permutation(jax.random.fold_in(rng, 2), count)[standing].astype(jnp.int32)


def gaussian(rng, extent, spread, reach, pieces=(), held_as=jnp.bfloat16):
    level = steps_of(rng, extent, pieces, -0.22, 0.18) if pieces else 1.0
    drawn = jax.random.normal(rng, extent, jnp.float32) * spread * level
    return jnp.minimum(jnp.maximum(drawn, -reach), reach).astype(held_as)


def setup_inputs(seed: int = 0) -> dict:
    arg_keys = jax.random.split(jax.random.key(seed), 5)
    return {
        "occ_irrep": touch_ends(ranked_ids(arg_keys[0], (OCC,), 8, 4), jax.random.fold_in(arg_keys[0], 3), 0, 7).astype(jnp.int32),
        "amplitudes": gaussian(arg_keys[1], (OPAIRS, VIRT * VIRT), 1.0, 6.0, ((0, 32), (1, 4))),
        "ladder_ints": gaussian(arg_keys[2], (VIRT * VIRT, VIRT * VIRT), (VIRT * VIRT) ** -0.5, 0.046875, ((0, 4), (1, 32))),
        "cycle_ints": gaussian(arg_keys[3], (OCC, VIRT, VIRT * OCC), (OCC * VIRT) ** -0.5, 0.03125, ((1, 4), (2, 32))),
    }


def reference(occ_irrep, amplitudes, ladder_ints, cycle_ints):
    row_index = jnp.arange(IWIN * OCC, dtype=jnp.int32)
    pair_first = row_index // OCC
    pair_second = row_index % OCC
    allowed = occ_irrep[pair_first] == occ_irrep[pair_second]
    amp_sym = jnp.where(allowed[:, None], amplitudes, jnp.zeros((), amplitudes.dtype))
    ladder = jnp.dot(amp_sym, ladder_ints, preferred_element_type=jnp.float32).reshape(IWIN, OCC, VIRT * VIRT)
    cycle_flat = cycle_ints.reshape(OCC * VIRT, VIRT * OCC)

    def cycle_one(amp_one):
        return jnp.dot(amp_one.reshape(OCC * VIRT, VIRT).T, cycle_flat, preferred_element_type=jnp.float32)

    cycle_term = lax.map(cycle_one, amp_sym.reshape(IWIN, OCC * VIRT * VIRT)).reshape(IWIN, VIRT, VIRT, OCC)
    same_irrep = (occ_irrep[:IWIN][:, None] == occ_irrep[None, :]).astype(jnp.float32)
    cycle_term = cycle_term * same_irrep[:, None, None, :]
    cycle_moved = jnp.transpose(cycle_term, (0, 3, 1, 2)).reshape(IWIN, OCC, VIRT * VIRT)
    return ladder + cycle_moved
```

```python
import functools
import jax
import jax.numpy as jnp
from jax import lax
from jax.experimental import pallas as pl
from jax.experimental.pallas import tpu as pltpu
from jax.sharding import Mesh, PartitionSpec as P

PAIR = ("z", "y", "core")
C_STEP = 4


def cycle_kernel(window, vir_full, vt_ref, g_ref, o_ref):
    step = pl.program_id(0)
    rows = vt_ref.shape[2]
    total = None
    for c in range(vt_ref.shape[0]):
        lanes = slice(c * vir_full, (c + 1) * vir_full)
        rhs = jnp.concatenate([g_ref[i * rows:(i + 1) * rows, lanes] for i in range(window)], axis=1)
        part = jnp.dot(vt_ref[c], rhs, preferred_element_type=jnp.float32)
        total = part if total is None else total + part

    @pl.when(step == 0)
    def _():
        o_ref[...] = total

    @pl.when(step > 0)
    def _():
        o_ref[...] += total


def cycle_matmul(vt, g, window, vir_full):
    vir_part, n_cols, rows = vt.shape
    steps = vir_part // C_STEP
    return pl.pallas_call(
        functools.partial(cycle_kernel, window, vir_full),
        out_shape=jax.ShapeDtypeStruct((n_cols, window * vir_full), jnp.float32),
        grid=(steps,),
        in_specs=[
            pl.BlockSpec((C_STEP, n_cols, rows), lambda s: (s, 0, 0)),
            pl.BlockSpec((g.shape[0], C_STEP * vir_full), lambda s: (0, s)),
        ],
        out_specs=pl.BlockSpec((n_cols, window * vir_full), lambda s: (0, 0)),
        compiler_params=pltpu.CompilerParams(dimension_semantics=("arbitrary",), vmem_limit_bytes=48 * 1024 * 1024),
    )(vt, g)


def body(occ_irrep, amplitudes, ladder_ints, cycle_ints):
    rows_local, cols_local = amplitudes.shape
    occ_count, vir_part, cycle_cols = cycle_ints.shape
    vir_full = cols_local // vir_part
    vir_local = cycle_cols // occ_count
    pad_rows = -(-rows_local // 16) * 16
    pidx = lax.axis_index(PAIR)
    global_row = pidx * rows_local + jnp.arange(rows_local, dtype=jnp.int32)
    allowed = occ_irrep[global_row // occ_count] == occ_irrep[global_row % occ_count]
    amp_sym = jnp.where(allowed[:, None], amplitudes, jnp.zeros((), amplitudes.dtype))
    amp_pad = jnp.pad(amp_sym, ((0, pad_rows - rows_local), (0, 0)))
    part = lax.all_gather(amp_pad, ("z", "y"), axis=0, tiled=False)
    gathered = lax.all_gather(part, "core", axis=1, tiled=False)
    n_blocks = gathered.shape[0] * gathered.shape[1]
    g2 = gathered.reshape(n_blocks * pad_rows, cols_local)
    total_rows = n_blocks * rows_local
    window = total_rows // occ_count
    per_i = n_blocks // window

    ladder = jnp.dot(g2, ladder_ints, preferred_element_type=jnp.float32)
    ladder = ladder.reshape(n_blocks, pad_rows, -1)[:, :rows_local, :]
    ladder = ladder.reshape(window, occ_count, vir_local * vir_full)

    v4 = cycle_ints.reshape(per_i, rows_local, vir_part, cycle_cols)
    v4 = jnp.pad(v4, ((0, 0), (0, pad_rows - rows_local), (0, 0), (0, 0)))
    vt = jnp.transpose(v4, (2, 3, 0, 1)).reshape(vir_part, cycle_cols, per_i * pad_rows)
    cyc = cycle_matmul(vt, g2, window, vir_full)
    cyc = cyc.reshape(vir_local, occ_count, window, vir_full)
    same_irrep = (occ_irrep[:window][:, None] == occ_irrep[None, :]).astype(jnp.float32)
    cyc = cyc * jnp.transpose(same_irrep)[None, :, :, None]
    cycle_term = jnp.transpose(cyc, (2, 3, 0, 1))
    regrouped = lax.all_to_all(cycle_term, PAIR, split_axis=1, concat_axis=2, tiled=True)
    rows_here = regrouped.shape[0]
    moved = jnp.transpose(regrouped, (0, 3, 1, 2)).reshape(rows_here, occ_count, vir_local * vir_full)
    combined = ladder + moved
    return lax.psum_scatter(combined, "x", scatter_dimension=0, tiled=True)


def solution(mesh):
    devs = mesh.devices
    n_pair, n_int = devs.shape
    fine = Mesh(devs.reshape(4, n_pair // 8, 2, n_int), ("z", "y", "core", "x"))
    placed = (P(), P(PAIR, "x"), P("x", PAIR), P(None, "x", PAIR))
    return jax.shard_map(body, mesh=fine, in_specs=placed, out_specs=P("x", None, PAIR), check_vma=False)
```

```python
import functools
import jax
import jax.numpy as jnp
from jax import lax
from jax.experimental import pallas as pl
from jax.experimental.pallas import tpu as pltpu
from jax.sharding import Mesh, PartitionSpec as P

PAIR = ("z", "y", "core")
C_STEP = 4


def cycle_kernel(window, vir_full, vt_ref, g_ref, o_ref):
    step = pl.program_id(0)
    rows = vt_ref.shape[2]
    total = None
    for c in range(vt_ref.shape[0]):
        lanes = slice(c * vir_full, (c + 1) * vir_full)
        rhs = jnp.concatenate([g_ref[i * rows:(i + 1) * rows, lanes] for i in range(window)], axis=1)
        part = jnp.dot(vt_ref[c], rhs, preferred_element_type=jnp.float32)
        total = part if total is None else total + part

    @pl.when(step == 0)
    def _():
        o_ref[...] = total

    @pl.when(step > 0)
    def _():
        o_ref[...] += total


def cycle_matmul(vt, g, window, vir_full):
    vir_part, n_cols, rows = vt.shape
    steps = vir_part // C_STEP
    return pl.pallas_call(
        functools.partial(cycle_kernel, window, vir_full),
        out_shape=jax.ShapeDtypeStruct((n_cols, window * vir_full), jnp.float32),
        grid=(steps,),
        in_specs=[
            pl.BlockSpec((C_STEP, n_cols, rows), lambda s: (s, 0, 0)),
            pl.BlockSpec((g.shape[0], C_STEP * vir_full), lambda s: (0, s)),
        ],
        out_specs=pl.BlockSpec((n_cols, window * vir_full), lambda s: (0, 0)),
        compiler_params=pltpu.CompilerParams(dimension_semantics=("arbitrary",), vmem_limit_bytes=48 * 1024 * 1024),
    )(vt, g)


def body(occ_irrep, amplitudes, ladder_ints, cycle_ints):
    rows_local, cols_local = amplitudes.shape
    occ_count, vir_part, cycle_cols = cycle_ints.shape
    vir_full = cols_local // vir_part
    vir_local = cycle_cols // occ_count
    pad_rows = -(-rows_local // 16) * 16
    pidx = lax.axis_index(PAIR)
    global_row = pidx * rows_local + jnp.arange(rows_local, dtype=jnp.int32)
    allowed = occ_irrep[global_row // occ_count] == occ_irrep[global_row % occ_count]
    amp_sym = jnp.where(allowed[:, None], amplitudes, jnp.zeros((), amplitudes.dtype))
    amp_pad = jnp.pad(amp_sym, ((0, pad_rows - rows_local), (0, 0)))
    g2 = lax.all_gather(amp_pad, PAIR, axis=0, tiled=True)
    n_blocks = g2.shape[0] // pad_rows
    total_rows = n_blocks * rows_local
    window = total_rows // occ_count
    per_i = n_blocks // window

    ladder = jnp.dot(g2, ladder_ints, preferred_element_type=jnp.float32)
    ladder = ladder.reshape(n_blocks, pad_rows, -1)[:, :rows_local, :]
    ladder = ladder.reshape(window, occ_count, vir_local * vir_full)

    v4 = cycle_ints.reshape(per_i, rows_local, vir_part, cycle_cols)
    v4 = jnp.pad(v4, ((0, 0), (0, pad_rows - rows_local), (0, 0), (0, 0)))
    vt = jnp.transpose(v4, (2, 3, 0, 1)).reshape(vir_part, cycle_cols, per_i * pad_rows)
    cyc = cycle_matmul(vt, g2, window, vir_full)
    cyc = cyc.reshape(vir_local, occ_count, window, vir_full)
    same_irrep = (occ_irrep[:window][:, None] == occ_irrep[None, :]).astype(jnp.float32)
    cyc = cyc * jnp.transpose(same_irrep)[None, :, :, None]
    cycle_term = jnp.transpose(cyc, (2, 3, 0, 1))
    regrouped = lax.all_to_all(cycle_term, PAIR, split_axis=1, concat_axis=2, tiled=True)
    rows_here = regrouped.shape[0]
    moved = jnp.transpose(regrouped, (0, 3, 1, 2)).reshape(rows_here, occ_count, vir_local * vir_full)
    combined = ladder + moved
    return lax.psum_scatter(combined, "x", scatter_dimension=0, tiled=True)


def solution(mesh):
    devs = mesh.devices
    n_pair, n_int = devs.shape
    fine = Mesh(devs.reshape(4, n_pair // 8, 2, n_int), ("z", "y", "core", "x"))
    placed = (P(), P(PAIR, "x"), P("x", PAIR), P(None, "x", PAIR))
    return jax.shard_map(body, mesh=fine, in_specs=placed, out_specs=P("x", None, PAIR), check_vma=False)
```

```python
import functools
import jax
import jax.numpy as jnp
from jax import lax
from jax.experimental import pallas as pl
from jax.experimental.pallas import tpu as pltpu
from jax.sharding import Mesh, PartitionSpec as P

PAIR = ("z", "y", "core")
C_STEP = 4


def cycle_kernel(window, vir_full, vt_ref, g_ref, o_ref):
    step = pl.program_id(0)
    rows = vt_ref.shape[2]
    total = None
    for c in range(vt_ref.shape[0]):
        lanes = slice(c * vir_full, (c + 1) * vir_full)
        rhs = jnp.concatenate([g_ref[i * rows:(i + 1) * rows, lanes] for i in range(window)], axis=1)
        part = jnp.dot(vt_ref[c], rhs, preferred_element_type=jnp.float32)
        total = part if total is None else total + part

    for i in range(window):
        piece = total[:, i * vir_full:(i + 1) * vir_full]

        @pl.when(step == 0)
        def _():
            o_ref[i] = piece

        @pl.when(step > 0)
        def _():
            o_ref[i] += piece


def cycle_matmul(vt, g, window, vir_full):
    vir_part, n_cols, rows = vt.shape
    steps = vir_part // C_STEP
    return pl.pallas_call(
        functools.partial(cycle_kernel, window, vir_full),
        out_shape=jax.ShapeDtypeStruct((window, n_cols, vir_full), jnp.float32),
        grid=(steps,),
        in_specs=[
            pl.BlockSpec((C_STEP, n_cols, rows), lambda s: (s, 0, 0)),
            pl.BlockSpec((g.shape[0], C_STEP * vir_full), lambda s: (0, s)),
        ],
        out_specs=pl.BlockSpec((window, n_cols, vir_full), lambda s: (0, 0, 0)),
        compiler_params=pltpu.CompilerParams(dimension_semantics=("arbitrary",), vmem_limit_bytes=48 * 1024 * 1024),
    )(vt, g)


def body(occ_irrep, amplitudes, ladder_ints, cycle_ints):
    rows_local, cols_local = amplitudes.shape
    occ_count, vir_part, cycle_cols = cycle_ints.shape
    vir_full = cols_local // vir_part
    vir_local = cycle_cols // occ_count
    pad_rows = -(-rows_local // 16) * 16
    pidx = lax.axis_index(PAIR)
    global_row = pidx * rows_local + jnp.arange(rows_local, dtype=jnp.int32)
    allowed = occ_irrep[global_row // occ_count] == occ_irrep[global_row % occ_count]
    amp_sym = jnp.where(allowed[:, None], amplitudes, jnp.zeros((), amplitudes.dtype))
    amp_pad = jnp.pad(amp_sym, ((0, pad_rows - rows_local), (0, 0)))
    g2 = lax.all_gather(amp_pad, PAIR, axis=0, tiled=True)
    n_blocks = g2.shape[0] // pad_rows
    total_rows = n_blocks * rows_local
    window = total_rows // occ_count
    per_i = n_blocks // window

    ladder = jnp.dot(g2, ladder_ints, preferred_element_type=jnp.float32)
    ladder = ladder.reshape(n_blocks, pad_rows, -1)[:, :rows_local, :]
    ladder = ladder.reshape(window, occ_count, vir_local * vir_full)

    v4 = cycle_ints.reshape(per_i, rows_local, vir_part, cycle_cols)
    v4 = jnp.pad(v4, ((0, 0), (0, pad_rows - rows_local), (0, 0), (0, 0)))
    vt = jnp.transpose(v4, (2, 3, 0, 1)).reshape(vir_part, cycle_cols, per_i * pad_rows)
    cyc = cycle_matmul(vt, g2, window, vir_full)
    same_irrep = (occ_irrep[:window][:, None] == occ_irrep[None, :]).astype(jnp.float32)
    cyc = cyc.reshape(window, vir_local, occ_count, vir_full) * same_irrep[:, None, :, None]
    cyc = lax.psum_scatter(cyc, "x", scatter_dimension=0, tiled=True)
    rows_here = cyc.shape[0]
    cycle_term = jnp.transpose(cyc, (0, 3, 1, 2))
    regrouped = lax.all_to_all(cycle_term, PAIR, split_axis=1, concat_axis=2, tiled=True)
    moved = jnp.transpose(regrouped, (0, 3, 1, 2)).reshape(rows_here, occ_count, vir_local * vir_full)
    ladder = lax.psum_scatter(ladder, "x", scatter_dimension=0, tiled=True)
    return ladder + moved


def solution(mesh):
    devs = mesh.devices
    n_pair, n_int = devs.shape
    fine = Mesh(devs.reshape(4, n_pair // 8, 2, n_int), ("z", "y", "core", "x"))
    placed = (P(), P(PAIR, "x"), P("x", PAIR), P(None, "x", PAIR))
    return jax.shard_map(body, mesh=fine, in_specs=placed, out_specs=P("x", None, PAIR), check_vma=False)
```

```python
import functools
import jax
import jax.numpy as jnp
from jax import lax
from jax.experimental import pallas as pl
from jax.experimental.pallas import tpu as pltpu
from jax.sharding import Mesh, PartitionSpec as P

PAIR = ("z", "y", "core")
C_STEP = 4


def cycle_kernel(vir_full, vt_ref, g_ref, o_ref):
    step = pl.program_id(0)
    n_i = g_ref.shape[0]
    total = None
    for c in range(vt_ref.shape[0]):
        lanes = slice(c * vir_full, (c + 1) * vir_full)
        rhs = jnp.concatenate([g_ref[q, :, lanes] for q in range(n_i)], axis=1)
        part = jnp.dot(vt_ref[c], rhs, preferred_element_type=jnp.float32)
        total = part if total is None else total + part
    for q in range(n_i):
        piece = total[:, q * vir_full:(q + 1) * vir_full]

        @pl.when(step == 0)
        def _():
            o_ref[q] = piece

        @pl.when(step > 0)
        def _():
            o_ref[q] += piece


def cycle_matmul(vt, g4, parity, vir_full):
    vir_part, n_cols, rows = vt.shape
    n_i = g4.shape[0]
    steps = vir_part // C_STEP
    return pl.pallas_call(
        functools.partial(cycle_kernel, vir_full),
        out_shape=jax.ShapeDtypeStruct((n_i, n_cols, vir_full), jnp.float32),
        grid=(steps,),
        in_specs=[
            pl.BlockSpec((C_STEP, n_cols, rows), lambda s: (s, 0, 0)),
            pl.BlockSpec((n_i, None, rows, C_STEP * vir_full), lambda s: (0, parity, 0, s)),
        ],
        out_specs=pl.BlockSpec((n_i, n_cols, vir_full), lambda s: (0, 0, 0)),
        compiler_params=pltpu.CompilerParams(dimension_semantics=("arbitrary",), vmem_limit_bytes=48 * 1024 * 1024),
    )(vt, g4)


def body(occ_irrep, amplitudes, ladder_ints, cycle_ints):
    rows_local, cols_local = amplitudes.shape
    occ_count, vir_part, cycle_cols = cycle_ints.shape
    vir_full = cols_local // vir_part
    vir_local = cycle_cols // occ_count
    pad_rows = -(-rows_local // 16) * 16
    per_i = occ_count // rows_local
    pidx = lax.axis_index(PAIR)
    label_first = lax.dynamic_slice(occ_irrep, (pidx // per_i,), (1,))
    label_second = lax.dynamic_slice(occ_irrep, ((pidx % per_i) * rows_local,), (rows_local,))
    allowed = label_first == label_second
    amp_sym = jnp.where(allowed[:, None], amplitudes, jnp.zeros((), amplitudes.dtype))
    amp_pad = jnp.pad(amp_sym, ((0, pad_rows - rows_local), (0, 0)))
    g2 = lax.all_gather(amp_pad, PAIR, axis=0, tiled=True)
    n_blocks = g2.shape[0] // pad_rows
    window = n_blocks // per_i
    n_x = lax.axis_size("x")
    i_here = window // n_x

    v4 = cycle_ints.reshape(per_i, rows_local, vir_part, cycle_cols)
    v4 = jnp.pad(v4, ((0, 0), (0, pad_rows - rows_local), (0, 0), (0, 0)))
    vt = jnp.transpose(v4, (2, 3, 0, 1)).reshape(vir_part, cycle_cols, per_i * pad_rows)
    g4 = g2.reshape(n_x, i_here, per_i * pad_rows, cols_local)
    same_irrep = (occ_irrep[:window][:, None] == occ_irrep[None, :]).astype(jnp.float32)
    same4 = same_irrep.reshape(n_x, i_here, occ_count)

    moved_parts = []
    for parity in range(i_here):
        cyc = cycle_matmul(vt, g4, parity, vir_full)
        cyc = cyc.reshape(n_x, vir_local, occ_count, vir_full) * same4[:, parity, None, :, None]
        cyc = lax.psum_scatter(cyc, "x", scatter_dimension=0, tiled=True)
        cycle_term = jnp.transpose(cyc, (0, 3, 1, 2))
        regrouped = lax.all_to_all(cycle_term, PAIR, split_axis=1, concat_axis=2, tiled=True)
        moved_parts.append(jnp.transpose(regrouped, (0, 3, 1, 2)).reshape(1, occ_count, vir_local * vir_full))

    ladder = jnp.dot(g2, ladder_ints, preferred_element_type=jnp.float32)
    ladder = ladder.reshape(n_blocks, pad_rows, -1)[:, :rows_local, :]
    ladder = ladder.reshape(window, occ_count, vir_local * vir_full)
    ladder = lax.psum_scatter(ladder, "x", scatter_dimension=0, tiled=True)
    return ladder + jnp.concatenate(moved_parts, axis=0)


def solution(mesh):
    devs = mesh.devices
    n_pair, n_int = devs.shape
    fine = Mesh(devs.reshape(4, n_pair // 8, 2, n_int), ("z", "y", "core", "x"))
    placed = (P(), P(PAIR, "x"), P("x", PAIR), P(None, "x", PAIR))
    return jax.shard_map(body, mesh=fine, in_specs=placed, out_specs=P("x", None, PAIR), check_vma=False)
```

```python
import functools
import jax
import jax.numpy as jnp
from jax import lax
from jax.experimental import pallas as pl
from jax.experimental.pallas import tpu as pltpu
from jax.sharding import Mesh, PartitionSpec as P

PAIR = ("z", "y", "core")
C_STEP = 4


def cycle_kernel(window, vir_full, vt_ref, g_ref, o_ref):
    step = pl.program_id(0)
    rows = vt_ref.shape[2]
    total = None
    for c in range(vt_ref.shape[0]):
        lanes = slice(c * vir_full, (c + 1) * vir_full)
        rhs = jnp.concatenate([g_ref[i * rows:(i + 1) * rows, lanes] for i in range(window)], axis=1)
        part = jnp.dot(vt_ref[c], rhs, preferred_element_type=jnp.float32)
        total = part if total is None else total + part

    for i in range(window):
        piece = total[:, i * vir_full:(i + 1) * vir_full]

        @pl.when(step == 0)
        def _():
            o_ref[i] = piece

        @pl.when(step > 0)
        def _():
            o_ref[i] += piece


def cycle_matmul(vt, g, window, vir_full):
    vir_part, n_cols, rows = vt.shape
    steps = vir_part // C_STEP
    return pl.pallas_call(
        functools.partial(cycle_kernel, window, vir_full),
        out_shape=jax.ShapeDtypeStruct((window, n_cols, vir_full), jnp.float32),
        grid=(steps,),
        in_specs=[
            pl.BlockSpec((C_STEP, n_cols, rows), lambda s: (s, 0, 0)),
            pl.BlockSpec((g.shape[0], C_STEP * vir_full), lambda s: (0, s)),
        ],
        out_specs=pl.BlockSpec((window, n_cols, vir_full), lambda s: (0, 0, 0)),
        compiler_params=pltpu.CompilerParams(dimension_semantics=("arbitrary",), vmem_limit_bytes=48 * 1024 * 1024),
    )(vt, g)


def ring_reduce_scatter(blocks, axis):
    n = lax.axis_size(axis)
    me = lax.axis_index(axis)
    per = blocks.shape[0] // n
    blocks = blocks.reshape((n, per) + blocks.shape[1:])
    half = per // 2
    lo, hi = blocks[:, :half], blocks[:, half:]
    fwd = [(j, (j + 1) % n) for j in range(n)]
    bwd = [(j, (j - 1) % n) for j in range(n)]
    acc_lo = lax.dynamic_index_in_dim(lo, (me - 1) % n, axis=0, keepdims=False)
    acc_hi = lax.dynamic_index_in_dim(hi, (me + 1) % n, axis=0, keepdims=False)
    for step in range(1, n):
        acc_lo = lax.ppermute(acc_lo, axis, fwd) + lax.dynamic_index_in_dim(lo, (me - 1 - step) % n, axis=0, keepdims=False)
        acc_hi = lax.ppermute(acc_hi, axis, bwd) + lax.dynamic_index_in_dim(hi, (me + 1 + step) % n, axis=0, keepdims=False)
    return jnp.concatenate([acc_lo, acc_hi], axis=0)


def body(occ_irrep, amplitudes, ladder_ints, cycle_ints):
    rows_local, cols_local = amplitudes.shape
    occ_count, vir_part, cycle_cols = cycle_ints.shape
    vir_full = cols_local // vir_part
    vir_local = cycle_cols // occ_count
    pad_rows = -(-rows_local // 16) * 16
    per_i = occ_count // rows_local
    pidx = lax.axis_index(PAIR)
    label_first = lax.dynamic_slice(occ_irrep, (pidx // per_i,), (1,))
    label_second = lax.dynamic_slice(occ_irrep, ((pidx % per_i) * rows_local,), (rows_local,))
    allowed = label_first == label_second
    amp_sym = jnp.where(allowed[:, None], amplitudes, jnp.zeros((), amplitudes.dtype))
    amp_pad = jnp.pad(amp_sym, ((0, pad_rows - rows_local), (0, 0)))
    g2 = lax.all_gather(amp_pad, PAIR, axis=0, tiled=True)
    n_blocks = g2.shape[0] // pad_rows
    total_rows = n_blocks * rows_local
    window = total_rows // occ_count

    ladder = jnp.dot(g2, ladder_ints, preferred_element_type=jnp.float32)
    ladder = ladder.reshape(n_blocks, pad_rows, -1)[:, :rows_local, :]
    ladder = ladder.reshape(window, occ_count, vir_local * vir_full)

    v4 = cycle_ints.reshape(per_i, rows_local, vir_part, cycle_cols)
    v4 = jnp.pad(v4, ((0, 0), (0, pad_rows - rows_local), (0, 0), (0, 0)))
    vt = jnp.transpose(v4, (2, 3, 0, 1)).reshape(vir_part, cycle_cols, per_i * pad_rows)
    cyc = cycle_matmul(vt, g2, window, vir_full)
    same_irrep = (occ_irrep[:window][:, None] == occ_irrep[None, :]).astype(jnp.float32)
    cyc = cyc.reshape(window, vir_local, occ_count, vir_full) * same_irrep[:, None, :, None]
    cyc = lax.psum_scatter(cyc, "x", scatter_dimension=0, tiled=True)
    rows_here = cyc.shape[0]
    cycle_term = jnp.transpose(cyc, (0, 3, 1, 2))
    regrouped = lax.all_to_all(cycle_term, PAIR, split_axis=1, concat_axis=2, tiled=True)
    moved = jnp.transpose(regrouped, (0, 3, 1, 2)).reshape(rows_here, occ_count, vir_local * vir_full)
    ladder = ring_reduce_scatter(ladder, "x")
    return ladder + moved


def solution(mesh):
    devs = mesh.devices
    n_pair, n_int = devs.shape
    fine = Mesh(devs.reshape(4, n_pair // 8, 2, n_int), ("z", "y", "core", "x"))
    placed = (P(), P(PAIR, "x"), P("x", PAIR), P(None, "x", PAIR))
    return jax.shard_map(body, mesh=fine, in_specs=placed, out_specs=P("x", None, PAIR), check_vma=False)
```

```python
import functools
import jax
import jax.numpy as jnp
from jax import lax
from jax.experimental import pallas as pl
from jax.experimental.pallas import tpu as pltpu
from jax.sharding import Mesh, PartitionSpec as P

PAIR = ("z", "y", "core")
C_STEP = 4
N_CHUNKS = 2


def cycle_kernel(window, vir_full, vt_ref, g_ref, *refs):
    o_ref = refs[-1]
    init_ref = refs[0] if len(refs) == 2 else None
    step = pl.program_id(0)
    rows = vt_ref.shape[2]
    total = None
    for c in range(vt_ref.shape[0]):
        lanes = slice(c * vir_full, (c + 1) * vir_full)
        rhs = jnp.concatenate([g_ref[i * rows:(i + 1) * rows, lanes] for i in range(window)], axis=1)
        part = jnp.dot(vt_ref[c], rhs, preferred_element_type=jnp.float32)
        total = part if total is None else total + part
    for i in range(window):
        piece = total[:, i * vir_full:(i + 1) * vir_full]

        @pl.when(step == 0)
        def _():
            if init_ref is None:
                o_ref[i] = piece
            else:
                o_ref[i] = init_ref[i] + piece

        @pl.when(step > 0)
        def _():
            o_ref[i] += piece


def cycle_matmul(vt, g, window, vir_full, init=None):
    vir_part, n_cols, rows = vt.shape
    steps = vir_part // C_STEP
    out_block = pl.BlockSpec((window, n_cols, vir_full), lambda s: (0, 0, 0))
    in_specs = [
        pl.BlockSpec((C_STEP, n_cols, rows), lambda s: (s, 0, 0)),
        pl.BlockSpec((g.shape[0], C_STEP * vir_full), lambda s: (0, s)),
    ]
    operands = [vt, g]
    aliases = {}
    if init is not None:
        in_specs.append(out_block)
        operands.append(init)
        aliases = {2: 0}
    return pl.pallas_call(
        functools.partial(cycle_kernel, window, vir_full),
        out_shape=jax.ShapeDtypeStruct((window, n_cols, vir_full), jnp.float32),
        grid=(steps,),
        in_specs=in_specs,
        out_specs=out_block,
        input_output_aliases=aliases,
        compiler_params=pltpu.CompilerParams(dimension_semantics=("arbitrary",), vmem_limit_bytes=48 * 1024 * 1024),
    )(*operands)


def body(occ_irrep, amplitudes, ladder_ints, cycle_ints):
    rows_local, cols_local = amplitudes.shape
    occ_count, vir_part, cycle_cols = cycle_ints.shape
    vir_full = cols_local // vir_part
    vir_local = cycle_cols // occ_count
    pad_rows = -(-rows_local // 16) * 16
    per_i = occ_count // rows_local
    pidx = lax.axis_index(PAIR)
    label_first = lax.dynamic_slice(occ_irrep, (pidx // per_i,), (1,))
    label_second = lax.dynamic_slice(occ_irrep, ((pidx % per_i) * rows_local,), (rows_local,))
    allowed = label_first == label_second
    amp_sym = jnp.where(allowed[:, None], amplitudes, jnp.zeros((), amplitudes.dtype))
    amp_pad = jnp.pad(amp_sym, ((0, pad_rows - rows_local), (0, 0)))
    chunk_cols = cols_local // N_CHUNKS
    chunk_c = vir_part // N_CHUNKS
    gathered = [
        lax.all_gather(amp_pad[:, q * chunk_cols:(q + 1) * chunk_cols], PAIR, axis=0, tiled=True)
        for q in range(N_CHUNKS)
    ]
    n_blocks = gathered[0].shape[0] // pad_rows
    total_rows = n_blocks * rows_local
    window = total_rows // occ_count

    v4 = cycle_ints.reshape(per_i, rows_local, vir_part, cycle_cols)
    v4 = jnp.pad(v4, ((0, 0), (0, pad_rows - rows_local), (0, 0), (0, 0)))
    vt = jnp.transpose(v4, (2, 3, 0, 1)).reshape(vir_part, cycle_cols, per_i * pad_rows)

    cyc = None
    ladder = None
    for q in range(N_CHUNKS):
        cyc = cycle_matmul(vt[q * chunk_c:(q + 1) * chunk_c], gathered[q], window, vir_full, cyc)
        part = jnp.dot(gathered[q], ladder_ints[q * chunk_cols:(q + 1) * chunk_cols],
                       preferred_element_type=jnp.float32)
        ladder = part if ladder is None else ladder + part

    same_irrep = (occ_irrep[:window][:, None] == occ_irrep[None, :]).astype(jnp.float32)
    cyc = cyc.reshape(window, vir_local, occ_count, vir_full) * same_irrep[:, None, :, None]
    cyc = lax.psum_scatter(cyc, "x", scatter_dimension=0, tiled=True)
    rows_here = cyc.shape[0]
    cycle_term = jnp.transpose(cyc, (0, 3, 1, 2))
    regrouped = lax.all_to_all(cycle_term, PAIR, split_axis=1, concat_axis=2, tiled=True)
    moved = jnp.transpose(regrouped, (0, 3, 1, 2)).reshape(rows_here, occ_count, vir_local * vir_full)

    ladder = ladder.reshape(n_blocks, pad_rows, -1)[:, :rows_local, :]
    ladder = ladder.reshape(window, occ_count, vir_local * vir_full)
    ladder = lax.psum_scatter(ladder, "x", scatter_dimension=0, tiled=True)
    return ladder + moved


def solution(mesh):
    devs = mesh.devices
    n_pair, n_int = devs.shape
    fine = Mesh(devs.reshape(4, n_pair // 8, 2, n_int), ("z", "y", "core", "x"))
    placed = (P(), P(PAIR, "x"), P("x", PAIR), P(None, "x", PAIR))
    return jax.shard_map(body, mesh=fine, in_specs=placed, out_specs=P("x", None, PAIR), check_vma=False)
```

```python
import functools
import jax
import jax.numpy as jnp
from jax import lax
from jax.experimental import pallas as pl
from jax.experimental.pallas import tpu as pltpu
from jax.sharding import Mesh, PartitionSpec as P

PAIR = ("z", "y", "core")
C_STEP = 8


def cycle_kernel(window, vir_full, vt_ref, g_ref, m_ref, o_ref):
    step = pl.program_id(0)
    last = pl.num_programs(0) - 1
    rows = vt_ref.shape[2]
    total = None
    for c in range(vt_ref.shape[0]):
        lanes = slice(c * vir_full, (c + 1) * vir_full)
        rhs = jnp.concatenate([g_ref[i * rows:(i + 1) * rows, lanes] for i in range(window)], axis=1)
        part = jnp.dot(vt_ref[c], rhs, preferred_element_type=jnp.float32)
        total = part if total is None else total + part

    for i in range(window):
        piece = total[:, i * vir_full:(i + 1) * vir_full]

        @pl.when(step == 0)
        def _():
            o_ref[i] = piece

        @pl.when(step > 0)
        def _():
            o_ref[i] += piece

        @pl.when(step == last)
        def _():
            o_ref[i] = o_ref[i] * m_ref[i]


def cycle_matmul(vt, g, mask, window, vir_full):
    vir_part, n_cols, rows = vt.shape
    steps = vir_part // C_STEP
    return pl.pallas_call(
        functools.partial(cycle_kernel, window, vir_full),
        out_shape=jax.ShapeDtypeStruct((window, n_cols, vir_full), jnp.float32),
        grid=(steps,),
        in_specs=[
            pl.BlockSpec((C_STEP, n_cols, rows), lambda s: (s, 0, 0)),
            pl.BlockSpec((g.shape[0], C_STEP * vir_full), lambda s: (0, s)),
            pl.BlockSpec(mask.shape, lambda s: (0, 0, 0)),
        ],
        out_specs=pl.BlockSpec((window, n_cols, vir_full), lambda s: (0, 0, 0)),
        compiler_params=pltpu.CompilerParams(dimension_semantics=("arbitrary",), vmem_limit_bytes=48 * 1024 * 1024),
    )(vt, g, mask)


def body(occ_irrep, amplitudes, ladder_ints, cycle_ints):
    rows_local, cols_local = amplitudes.shape
    occ_count, vir_part, cycle_cols = cycle_ints.shape
    vir_full = cols_local // vir_part
    vir_local = cycle_cols // occ_count
    pad_rows = -(-rows_local // 16) * 16
    per_i = occ_count // rows_local
    pidx = lax.axis_index(PAIR)
    label_first = lax.dynamic_slice(occ_irrep, (pidx // per_i,), (1,))
    label_second = lax.dynamic_slice(occ_irrep, ((pidx % per_i) * rows_local,), (rows_local,))
    allowed = label_first == label_second
    amp_sym = jnp.where(allowed[:, None], amplitudes, jnp.zeros((), amplitudes.dtype))
    amp_pad = jnp.pad(amp_sym, ((0, pad_rows - rows_local), (0, 0)))
    g2 = lax.all_gather(amp_pad, PAIR, axis=0, tiled=True)
    n_blocks = g2.shape[0] // pad_rows
    total_rows = n_blocks * rows_local
    window = total_rows // occ_count

    ladder = jnp.dot(g2, ladder_ints, preferred_element_type=jnp.float32)
    ladder = ladder.reshape(n_blocks, pad_rows, -1)[:, :rows_local, :]
    ladder = ladder.reshape(window, occ_count, vir_local * vir_full)

    v4 = cycle_ints.reshape(per_i, rows_local, vir_part, cycle_cols)
    v4 = jnp.pad(v4, ((0, 0), (0, pad_rows - rows_local), (0, 0), (0, 0)))
    vt = jnp.transpose(v4, (2, 3, 0, 1)).reshape(vir_part, cycle_cols, per_i * pad_rows)
    same_irrep = (occ_irrep[:window][:, None] == occ_irrep[None, :]).astype(jnp.float32)
    mask = jnp.broadcast_to(same_irrep[:, None, :], (window, vir_local, occ_count)).reshape(window, cycle_cols, 1)
    cyc = cycle_matmul(vt, g2, mask, window, vir_full)
    cyc = cyc.reshape(window, vir_local, occ_count, vir_full)
    cyc = lax.psum_scatter(cyc, "x", scatter_dimension=0, tiled=True)
    rows_here = cyc.shape[0]
    cycle_term = jnp.transpose(cyc, (0, 3, 1, 2))
    regrouped = lax.all_to_all(cycle_term, PAIR, split_axis=1, concat_axis=2, tiled=True)
    moved = jnp.transpose(regrouped, (0, 3, 1, 2)).reshape(rows_here, occ_count, vir_local * vir_full)
    ladder = lax.psum_scatter(ladder, "x", scatter_dimension=0, tiled=True)
    return ladder + moved


def solution(mesh):
    devs = mesh.devices
    n_pair, n_int = devs.shape
    fine = Mesh(devs.reshape(4, n_pair // 8, 2, n_int), ("z", "y", "core", "x"))
    placed = (P(), P(PAIR, "x"), P("x", PAIR), P(None, "x", PAIR))
    return jax.shard_map(body, mesh=fine, in_specs=placed, out_specs=P("x", None, PAIR), check_vma=False)
```

```python
import functools
import jax
import jax.numpy as jnp
from jax import lax
from jax.experimental import pallas as pl
from jax.experimental.pallas import tpu as pltpu
from jax.sharding import Mesh, PartitionSpec as P

PAIR = ("z", "y", "core")
C_STEP = 4


def cycle_kernel(window, vir_full, vt_ref, g_ref, o_ref):
    step = pl.program_id(0)
    rows = vt_ref.shape[2]
    lhs = jnp.concatenate([vt_ref[c] for c in range(vt_ref.shape[0])], axis=1)
    rhs = jnp.concatenate(
        [
            jnp.concatenate(
                [g_ref[i * rows:(i + 1) * rows, c * vir_full:(c + 1) * vir_full] for i in range(window)], axis=1
            )
            for c in range(vt_ref.shape[0])
        ],
        axis=0,
    )
    total = jnp.dot(lhs, rhs, preferred_element_type=jnp.float32)
    for i in range(window):
        piece = total[:, i * vir_full:(i + 1) * vir_full]

        @pl.when(step == 0)
        def _():
            o_ref[i] = piece

        @pl.when(step > 0)
        def _():
            o_ref[i] += piece


def cycle_matmul(vt, g, window, vir_full):
    vir_part, n_cols, rows = vt.shape
    steps = vir_part // C_STEP
    return pl.pallas_call(
        functools.partial(cycle_kernel, window, vir_full),
        out_shape=jax.ShapeDtypeStruct((window, n_cols, vir_full), jnp.float32),
        grid=(steps,),
        in_specs=[
            pl.BlockSpec((C_STEP, n_cols, rows), lambda s: (s, 0, 0)),
            pl.BlockSpec((g.shape[0], C_STEP * vir_full), lambda s: (0, s)),
        ],
        out_specs=pl.BlockSpec((window, n_cols, vir_full), lambda s: (0, 0, 0)),
        compiler_params=pltpu.CompilerParams(dimension_semantics=("arbitrary",), vmem_limit_bytes=48 * 1024 * 1024),
    )(vt, g)


def body(occ_irrep, amplitudes, ladder_ints, cycle_ints):
    rows_local, cols_local = amplitudes.shape
    occ_count, vir_part, cycle_cols = cycle_ints.shape
    vir_full = cols_local // vir_part
    vir_local = cycle_cols // occ_count
    pad_rows = -(-rows_local // 16) * 16
    pidx = lax.axis_index(PAIR)
    global_row = pidx * rows_local + jnp.arange(rows_local, dtype=jnp.int32)
    allowed = occ_irrep[global_row // occ_count] == occ_irrep[global_row % occ_count]
    amp_sym = jnp.where(allowed[:, None], amplitudes, jnp.zeros((), amplitudes.dtype))
    amp_pad = jnp.pad(amp_sym, ((0, pad_rows - rows_local), (0, 0)))
    g2 = lax.all_gather(amp_pad, PAIR, axis=0, tiled=True)
    n_blocks = g2.shape[0] // pad_rows
    total_rows = n_blocks * rows_local
    window = total_rows // occ_count
    per_i = n_blocks // window

    ladder = jnp.dot(g2, ladder_ints, preferred_element_type=jnp.float32)
    ladder = ladder.reshape(n_blocks, pad_rows, -1)[:, :rows_local, :]
    ladder = ladder.reshape(window, occ_count, vir_local * vir_full)

    v4 = cycle_ints.reshape(per_i, rows_local, vir_part, cycle_cols)
    v4 = jnp.pad(v4, ((0, 0), (0, pad_rows - rows_local), (0, 0), (0, 0)))
    vt = jnp.transpose(v4, (2, 3, 0, 1)).reshape(vir_part, cycle_cols, per_i * pad_rows)
    cyc = cycle_matmul(vt, g2, window, vir_full)
    same_irrep = (occ_irrep[:window][:, None] == occ_irrep[None, :]).astype(jnp.float32)
    cyc = cyc.reshape(window, vir_local, occ_count, vir_full) * same_irrep[:, None, :, None]
    cyc = lax.psum_scatter(cyc, "x", scatter_dimension=0, tiled=True)
    rows_here = cyc.shape[0]
    cycle_term = jnp.transpose(cyc, (0, 3, 1, 2))
    regrouped = lax.all_to_all(cycle_term, PAIR, split_axis=1, concat_axis=2, tiled=True)
    moved = jnp.transpose(regrouped, (0, 3, 1, 2)).reshape(rows_here, occ_count, vir_local * vir_full)
    ladder = lax.psum_scatter(ladder, "x", scatter_dimension=0, tiled=True)
    return ladder + moved


def solution(mesh):
    devs = mesh.devices
    n_pair, n_int = devs.shape
    fine = Mesh(devs.reshape(4, n_pair // 8, 2, n_int), ("z", "y", "core", "x"))
    placed = (P(), P(PAIR, "x"), P("x", PAIR), P(None, "x", PAIR))
    return jax.shard_map(body, mesh=fine, in_specs=placed, out_specs=P("x", None, PAIR), check_vma=False)
```

```python
import functools
import jax
import jax.numpy as jnp
from jax import lax
from jax.experimental import pallas as pl
from jax.experimental.pallas import tpu as pltpu
from jax.sharding import Mesh, PartitionSpec as P

PAIR = ("z", "y", "core")
C_STEP = 4


def cycle_kernel(window, vir_full, vt_ref, g_ref, o_ref):
    step = pl.program_id(0)
    rows = vt_ref.shape[2]
    total = None
    for c in range(vt_ref.shape[0]):
        lanes = slice(c * vir_full, (c + 1) * vir_full)
        rhs = jnp.concatenate([g_ref[i * rows:(i + 1) * rows, lanes] for i in range(window)], axis=1)
        part = jnp.dot(vt_ref[c], rhs, preferred_element_type=jnp.float32)
        total = part if total is None else total + part

    for i in range(window):
        piece = total[:, i * vir_full:(i + 1) * vir_full]

        @pl.when(step == 0)
        def _():
            o_ref[i] = piece

        @pl.when(step > 0)
        def _():
            o_ref[i] += piece


def cycle_matmul(vt, g, window, vir_full):
    vir_part, n_cols, rows = vt.shape
    steps = vir_part // C_STEP
    return pl.pallas_call(
        functools.partial(cycle_kernel, window, vir_full),
        out_shape=jax.ShapeDtypeStruct((window, n_cols, vir_full), jnp.float32),
        grid=(steps,),
        in_specs=[
            pl.BlockSpec((C_STEP, n_cols, rows), lambda s: (s, 0, 0)),
            pl.BlockSpec((g.shape[0], C_STEP * vir_full), lambda s: (0, s)),
        ],
        out_specs=pl.BlockSpec((window, n_cols, vir_full), lambda s: (0, 0, 0)),
        compiler_params=pltpu.CompilerParams(dimension_semantics=("arbitrary",), vmem_limit_bytes=48 * 1024 * 1024),
    )(vt, g)


def body(occ_irrep, amplitudes, ladder_ints, cycle_ints):
    rows_local, cols_local = amplitudes.shape
    occ_count, vir_part, cycle_cols = cycle_ints.shape
    vir_full = cols_local // vir_part
    vir_local = cycle_cols // occ_count
    pad_rows = -(-rows_local // 16) * 16
    pidx = lax.axis_index(PAIR)
    per_i = occ_count // rows_local
    labels = jnp.concatenate([occ_irrep, jnp.full((pad_rows - rows_local,), -1, occ_irrep.dtype)])
    label_first = lax.dynamic_slice(occ_irrep, (pidx // per_i,), (1,))
    label_second = lax.dynamic_slice(labels, ((pidx % per_i) * rows_local,), (pad_rows,))
    row = lax.broadcasted_iota(jnp.int32, (pad_rows,), 0)
    allowed = (label_second == label_first) & (row < rows_local)
    amp_pad = jnp.where(allowed[:, None], jnp.pad(amplitudes, ((0, pad_rows - rows_local), (0, 0))),
                        jnp.zeros((), amplitudes.dtype))
    g2 = lax.all_gather(amp_pad, PAIR, axis=0, tiled=True)
    n_blocks = g2.shape[0] // pad_rows
    total_rows = n_blocks * rows_local
    window = total_rows // occ_count

    ladder = jnp.dot(g2, ladder_ints, preferred_element_type=jnp.float32)
    ladder = ladder.reshape(n_blocks, pad_rows, -1)[:, :rows_local, :]
    ladder = ladder.reshape(window, occ_count, vir_local * vir_full)

    v4 = cycle_ints.reshape(per_i, rows_local, vir_part, cycle_cols)
    v4 = jnp.pad(v4, ((0, 0), (0, pad_rows - rows_local), (0, 0), (0, 0)))
    vt = jnp.transpose(v4, (2, 3, 0, 1)).reshape(vir_part, cycle_cols, per_i * pad_rows)
    cyc = cycle_matmul(vt, g2, window, vir_full)
    same_irrep = (occ_irrep[:window][:, None] == occ_irrep[None, :]).astype(jnp.float32)
    cyc = cyc.reshape(window, vir_local, occ_count, vir_full) * same_irrep[:, None, :, None]
    cyc = lax.psum_scatter(cyc, "x", scatter_dimension=0, tiled=True)
    rows_here = cyc.shape[0]
    cycle_term = jnp.transpose(cyc, (0, 3, 1, 2))
    regrouped = lax.all_to_all(cycle_term, PAIR, split_axis=1, concat_axis=2, tiled=True)
    moved = jnp.transpose(regrouped, (0, 3, 1, 2)).reshape(rows_here, occ_count, vir_local * vir_full)
    ladder = lax.psum_scatter(ladder, "x", scatter_dimension=0, tiled=True)
    return ladder + moved


def solution(mesh):
    devs = mesh.devices
    n_pair, n_int = devs.shape
    fine = Mesh(devs.reshape(4, n_pair // 8, 2, n_int), ("z", "y", "core", "x"))
    placed = (P(), P(PAIR, "x"), P("x", PAIR), P(None, "x", PAIR))
    return jax.shard_map(body, mesh=fine, in_specs=placed, out_specs=P("x", None, PAIR), check_vma=False)
```

```python
import functools
import jax
import jax.numpy as jnp
from jax import lax
from jax.experimental import pallas as pl
from jax.experimental.pallas import tpu as pltpu
from jax.sharding import Mesh, PartitionSpec as P

PAIR = ("z", "y", "core")
C_STEP = 4


def cycle_kernel(vir_full, vt_ref, g_ref, *refs):
    o_ref = refs[-1]
    step = pl.program_id(0)
    n_i = g_ref.shape[0]
    total = None
    for c in range(vt_ref.shape[0]):
        lanes = slice(c * vir_full, (c + 1) * vir_full)
        rhs = jnp.concatenate([g_ref[q, :, lanes] for q in range(n_i)], axis=1)
        part = jnp.dot(vt_ref[c], rhs, preferred_element_type=jnp.float32)
        total = part if total is None else total + part
    for q in range(n_i):
        piece = total[:, q * vir_full:(q + 1) * vir_full]

        @pl.when(step == 0)
        def _():
            o_ref[q] = piece

        @pl.when(step > 0)
        def _():
            o_ref[q] += piece


def cycle_matmul(vt, g4, parity, vir_full, after=None):
    vir_part, n_cols, rows = vt.shape
    n_i = g4.shape[0]
    steps = vir_part // C_STEP
    return pl.pallas_call(
        functools.partial(cycle_kernel, vir_full),
        out_shape=jax.ShapeDtypeStruct((n_i, n_cols, vir_full), jnp.float32),
        grid=(steps,),
        in_specs=[
            pl.BlockSpec((C_STEP, n_cols, rows), lambda s: (s, 0, 0)),
            pl.BlockSpec((n_i, None, rows, C_STEP * vir_full), lambda s: (0, parity, 0, s)),
        ] + ([] if after is None else [pl.BlockSpec(memory_space=pl.ANY)]),
        out_specs=pl.BlockSpec((n_i, n_cols, vir_full), lambda s: (0, 0, 0)),
        compiler_params=pltpu.CompilerParams(dimension_semantics=("arbitrary",), vmem_limit_bytes=48 * 1024 * 1024),
    )(vt, g4, *([] if after is None else [after]))


def body(occ_irrep, amplitudes, ladder_ints, cycle_ints):
    rows_local, cols_local = amplitudes.shape
    occ_count, vir_part, cycle_cols = cycle_ints.shape
    vir_full = cols_local // vir_part
    vir_local = cycle_cols // occ_count
    pad_rows = -(-rows_local // 16) * 16
    per_i = occ_count // rows_local
    pidx = lax.axis_index(PAIR)
    label_first = lax.dynamic_slice(occ_irrep, (pidx // per_i,), (1,))
    label_second = lax.dynamic_slice(occ_irrep, ((pidx % per_i) * rows_local,), (rows_local,))
    allowed = label_first == label_second
    amp_sym = jnp.where(allowed[:, None], amplitudes, jnp.zeros((), amplitudes.dtype))
    amp_pad = jnp.pad(amp_sym, ((0, pad_rows - rows_local), (0, 0)))
    g2 = lax.all_gather(amp_pad, PAIR, axis=0, tiled=True)
    n_blocks = g2.shape[0] // pad_rows
    window = n_blocks // per_i
    n_x = lax.axis_size("x")
    i_here = window // n_x

    v4 = cycle_ints.reshape(per_i, rows_local, vir_part, cycle_cols)
    v4 = jnp.pad(v4, ((0, 0), (0, pad_rows - rows_local), (0, 0), (0, 0)))
    vt = jnp.transpose(v4, (2, 3, 0, 1)).reshape(vir_part, cycle_cols, per_i * pad_rows)
    g4 = g2.reshape(n_x, i_here, per_i * pad_rows, cols_local)
    same_irrep = (occ_irrep[:window][:, None] == occ_irrep[None, :]).astype(jnp.float32)
    same4 = same_irrep.reshape(n_x, i_here, occ_count)

    def masked(parity, after=None):
        cyc = cycle_matmul(vt, g4, parity, vir_full, after)
        return cyc.reshape(n_x, vir_local, occ_count, vir_full) * same4[:, parity, None, :, None]

    def regroup(cycle_term):
        regrouped = lax.all_to_all(cycle_term, PAIR, split_axis=1, concat_axis=2, tiled=True)
        return jnp.transpose(regrouped, (0, 3, 1, 2)).reshape(cycle_term.shape[0], occ_count, vir_local * vir_full)

    term_even = jnp.transpose(masked(0), (0, 3, 1, 2))
    moved_even = regroup(term_even)
    odd = lax.psum_scatter(masked(1, term_even), "x", scatter_dimension=0, tiled=True)
    moved_odd = regroup(jnp.transpose(odd, (0, 3, 1, 2)))

    ladder = jnp.dot(g2, ladder_ints, preferred_element_type=jnp.float32)
    ladder = ladder.reshape(n_blocks, pad_rows, -1)[:, :rows_local, :]
    ladder = ladder.reshape(n_x, i_here, occ_count, vir_local * vir_full)
    ladder = ladder.at[:, 0].add(moved_even).reshape(window, occ_count, vir_local * vir_full)
    ladder = lax.psum_scatter(ladder, "x", scatter_dimension=0, tiled=True)
    return ladder.at[1:].add(moved_odd)


def solution(mesh):
    devs = mesh.devices
    n_pair, n_int = devs.shape
    fine = Mesh(devs.reshape(4, n_pair // 8, 2, n_int), ("z", "y", "core", "x"))
    placed = (P(), P(PAIR, "x"), P("x", PAIR), P(None, "x", PAIR))
    return jax.shard_map(body, mesh=fine, in_specs=placed, out_specs=P("x", None, PAIR), check_vma=False)
```

```python
import functools
import jax
import jax.numpy as jnp
from jax import lax
from jax.experimental import pallas as pl
from jax.experimental.pallas import tpu as pltpu
from jax.sharding import Mesh, PartitionSpec as P

PAIR = ("z", "y", "core")
C_STEP = 4


def cycle_kernel(window, vir_full, vt_ref, g_ref, m_ref, o_ref):
    step = pl.program_id(0)
    last = pl.num_programs(0) - 1
    rows = vt_ref.shape[2]
    total = None
    for c in range(vt_ref.shape[0]):
        lanes = slice(c * vir_full, (c + 1) * vir_full)
        rhs = jnp.concatenate([g_ref[i * rows:(i + 1) * rows, lanes] for i in range(window)], axis=1)
        part = jnp.dot(vt_ref[c], rhs, preferred_element_type=jnp.float32)
        total = part if total is None else total + part

    for i in range(window):
        piece = total[:, i * vir_full:(i + 1) * vir_full]

        @pl.when(step == 0)
        def _():
            o_ref[i] = piece

        @pl.when(step > 0)
        def _():
            o_ref[i] += piece

        @pl.when(step == last)
        def _():
            o_ref[i] = o_ref[i] * m_ref[i]


def cycle_matmul(vt, g, mask, window, vir_full):
    vir_part, n_cols, rows = vt.shape
    steps = vir_part // C_STEP
    return pl.pallas_call(
        functools.partial(cycle_kernel, window, vir_full),
        out_shape=jax.ShapeDtypeStruct((window, n_cols, vir_full), jnp.float32),
        grid=(steps,),
        in_specs=[
            pl.BlockSpec((C_STEP, n_cols, rows), lambda s: (s, 0, 0)),
            pl.BlockSpec((g.shape[0], C_STEP * vir_full), lambda s: (0, s)),
            pl.BlockSpec(mask.shape, lambda s: (0, 0, 0)),
        ],
        out_specs=pl.BlockSpec((window, n_cols, vir_full), lambda s: (0, 0, 0)),
        compiler_params=pltpu.CompilerParams(dimension_semantics=("arbitrary",), vmem_limit_bytes=48 * 1024 * 1024),
    )(vt, g, mask)


def body(occ_irrep, amplitudes, ladder_ints, cycle_ints):
    rows_local, cols_local = amplitudes.shape
    occ_count, vir_part, cycle_cols = cycle_ints.shape
    vir_full = cols_local // vir_part
    vir_local = cycle_cols // occ_count
    pad_rows = -(-rows_local // 16) * 16
    pidx = lax.axis_index(PAIR)
    per_i = occ_count // rows_local
    labels = jnp.concatenate([occ_irrep, jnp.full((pad_rows - rows_local,), -1, occ_irrep.dtype)])
    label_first = lax.dynamic_slice(occ_irrep, (pidx // per_i,), (1,))
    label_second = lax.dynamic_slice(labels, ((pidx % per_i) * rows_local,), (pad_rows,))
    row = lax.broadcasted_iota(jnp.int32, (pad_rows,), 0)
    allowed = (label_second == label_first) & (row < rows_local)
    amp_pad = jnp.where(allowed[:, None], jnp.pad(amplitudes, ((0, pad_rows - rows_local), (0, 0))),
                        jnp.zeros((), amplitudes.dtype))
    g2 = lax.all_gather(amp_pad, PAIR, axis=0, tiled=True)
    n_blocks = g2.shape[0] // pad_rows
    total_rows = n_blocks * rows_local
    window = total_rows // occ_count

    ladder = jnp.dot(g2, ladder_ints, preferred_element_type=jnp.float32)
    ladder = ladder.reshape(n_blocks, pad_rows, -1)[:, :rows_local, :]
    ladder = ladder.reshape(window, occ_count, vir_local * vir_full)

    v4 = cycle_ints.reshape(per_i, rows_local, vir_part, cycle_cols)
    v4 = jnp.pad(v4, ((0, 0), (0, pad_rows - rows_local), (0, 0), (0, 0)))
    vt = jnp.transpose(v4, (2, 3, 0, 1)).reshape(vir_part, cycle_cols, per_i * pad_rows)
    same_irrep = (occ_irrep[:window][:, None] == occ_irrep[None, :]).astype(jnp.float32)
    mask = jnp.broadcast_to(same_irrep[:, None, :], (window, vir_local, occ_count)).reshape(window, cycle_cols, 1)
    cyc = cycle_matmul(vt, g2, mask, window, vir_full)
    cyc = cyc.reshape(window, vir_local, occ_count, vir_full)
    cyc = lax.psum_scatter(cyc, "x", scatter_dimension=0, tiled=True)
    rows_here = cyc.shape[0]
    cycle_term = jnp.transpose(cyc, (0, 3, 1, 2))
    regrouped = lax.all_to_all(cycle_term, PAIR, split_axis=1, concat_axis=2, tiled=True)
    moved = jnp.transpose(regrouped, (0, 3, 1, 2)).reshape(rows_here, occ_count, vir_local * vir_full)
    ladder = lax.psum_scatter(ladder, "x", scatter_dimension=0, tiled=True)
    return ladder + moved


def solution(mesh):
    devs = mesh.devices
    n_pair, n_int = devs.shape
    fine = Mesh(devs.reshape(4, n_pair // 8, 2, n_int), ("z", "y", "core", "x"))
    placed = (P(), P(PAIR, "x"), P("x", PAIR), P(None, "x", PAIR))
    return jax.shard_map(body, mesh=fine, in_specs=placed, out_specs=P("x", None, PAIR), check_vma=False)
```

```python
import functools
import jax
import jax.numpy as jnp
from jax import lax
from jax.experimental import pallas as pl
from jax.experimental.pallas import tpu as pltpu
from jax.sharding import Mesh, PartitionSpec as P

PAIR = ("z", "y", "core")
C_STEP = 2


def cycle_kernel(window, vir_full, vt_ref, g_ref, o_ref):
    step = pl.program_id(0)
    rows = vt_ref.shape[2]
    total = None
    for c in range(vt_ref.shape[0]):
        lanes = slice(c * vir_full, (c + 1) * vir_full)
        rhs = jnp.concatenate([g_ref[i * rows:(i + 1) * rows, lanes] for i in range(window)], axis=1)
        part = jnp.dot(vt_ref[c], rhs, preferred_element_type=jnp.float32)
        total = part if total is None else total + part

    for i in range(window):
        piece = total[:, i * vir_full:(i + 1) * vir_full]

        @pl.when(step == 0)
        def _():
            o_ref[i] = piece

        @pl.when(step > 0)
        def _():
            o_ref[i] += piece


def cycle_matmul(vt, g, window, vir_full):
    vir_part, n_cols, rows = vt.shape
    steps = vir_part // C_STEP
    return pl.pallas_call(
        functools.partial(cycle_kernel, window, vir_full),
        out_shape=jax.ShapeDtypeStruct((window, n_cols, vir_full), jnp.float32),
        grid=(steps,),
        in_specs=[
            pl.BlockSpec((C_STEP, n_cols, rows), lambda s: (s, 0, 0)),
            pl.BlockSpec((g.shape[0], C_STEP * vir_full), lambda s: (0, s)),
        ],
        out_specs=pl.BlockSpec((window, n_cols, vir_full), lambda s: (0, 0, 0)),
        compiler_params=pltpu.CompilerParams(dimension_semantics=("arbitrary",), vmem_limit_bytes=48 * 1024 * 1024),
    )(vt, g)


def body(occ_irrep, amplitudes, ladder_ints, cycle_ints):
    rows_local, cols_local = amplitudes.shape
    occ_count, vir_part, cycle_cols = cycle_ints.shape
    vir_full = cols_local // vir_part
    vir_local = cycle_cols // occ_count
    pad_rows = -(-rows_local // 16) * 16
    pidx = lax.axis_index(PAIR)
    per_i = occ_count // rows_local
    labels = jnp.concatenate([occ_irrep, jnp.full((pad_rows - rows_local,), -1, occ_irrep.dtype)])
    label_first = lax.dynamic_slice(occ_irrep, (pidx // per_i,), (1,))
    label_second = lax.dynamic_slice(labels, ((pidx % per_i) * rows_local,), (pad_rows,))
    row = lax.broadcasted_iota(jnp.int32, (pad_rows,), 0)
    allowed = (label_second == label_first) & (row < rows_local)
    amp_pad = jnp.where(allowed[:, None], jnp.pad(amplitudes, ((0, pad_rows - rows_local), (0, 0))),
                        jnp.zeros((), amplitudes.dtype))
    g2 = lax.all_gather(amp_pad, PAIR, axis=0, tiled=True)
    n_blocks = g2.shape[0] // pad_rows
    total_rows = n_blocks * rows_local
    window = total_rows // occ_count

    ladder = jnp.dot(g2, ladder_ints, preferred_element_type=jnp.float32)
    ladder = ladder.reshape(n_blocks, pad_rows, -1)[:, :rows_local, :]
    ladder = ladder.reshape(window, occ_count, vir_local * vir_full)

    v4 = cycle_ints.reshape(per_i, rows_local, vir_part, cycle_cols)
    v4 = jnp.pad(v4, ((0, 0), (0, pad_rows - rows_local), (0, 0), (0, 0)))
    vt = jnp.transpose(v4, (2, 3, 0, 1)).reshape(vir_part, cycle_cols, per_i * pad_rows)
    cyc = cycle_matmul(vt, g2, window, vir_full)
    same_irrep = (occ_irrep[:window][:, None] == occ_irrep[None, :]).astype(jnp.float32)
    cyc = cyc.reshape(window, vir_local, occ_count, vir_full) * same_irrep[:, None, :, None]
    cyc = lax.psum_scatter(cyc, "x", scatter_dimension=0, tiled=True)
    rows_here = cyc.shape[0]
    cycle_term = jnp.transpose(cyc, (0, 3, 1, 2))
    regrouped = lax.all_to_all(cycle_term, PAIR, split_axis=1, concat_axis=2, tiled=True)
    moved = jnp.transpose(regrouped, (0, 3, 1, 2)).reshape(rows_here, occ_count, vir_local * vir_full)
    ladder = lax.psum_scatter(ladder, "x", scatter_dimension=0, tiled=True)
    return ladder + moved


def solution(mesh):
    devs = mesh.devices
    n_pair, n_int = devs.shape
    fine = Mesh(devs.reshape(4, n_pair // 8, 2, n_int), ("z", "y", "core", "x"))
    placed = (P(), P(PAIR, "x"), P("x", PAIR), P(None, "x", PAIR))
    return jax.shard_map(body, mesh=fine, in_specs=placed, out_specs=P("x", None, PAIR), check_vma=False)
```

```python
import functools
import jax
import jax.numpy as jnp
from jax import lax
from jax.experimental import pallas as pl
from jax.experimental.pallas import tpu as pltpu
from jax.sharding import Mesh, PartitionSpec as P

PAIR = ("z", "y", "core")
C_STEP = 4


def cycle_kernel(window, vir_full, vt_ref, g_ref, o_ref):
    step = pl.program_id(0)
    rows = vt_ref.shape[2]
    total = None
    for c in range(vt_ref.shape[0]):
        lanes = slice(c * vir_full, (c + 1) * vir_full)
        rhs = jnp.concatenate([g_ref[i * rows:(i + 1) * rows, lanes] for i in range(window)], axis=1)
        part = jnp.dot(vt_ref[c], rhs, preferred_element_type=jnp.float32)
        total = part if total is None else total + part

    for i in range(window):
        piece = total[:, i * vir_full:(i + 1) * vir_full]

        @pl.when(step == 0)
        def _():
            o_ref[i] = piece

        @pl.when(step > 0)
        def _():
            o_ref[i] += piece


def cycle_matmul(vt, g, window, vir_full):
    vir_part, n_cols, rows = vt.shape
    steps = vir_part // C_STEP
    return pl.pallas_call(
        functools.partial(cycle_kernel, window, vir_full),
        out_shape=jax.ShapeDtypeStruct((window, n_cols, vir_full), jnp.float32),
        grid=(steps,),
        in_specs=[
            pl.BlockSpec((C_STEP, n_cols, rows), lambda s: (s, 0, 0)),
            pl.BlockSpec((g.shape[0], C_STEP * vir_full), lambda s: (0, s)),
        ],
        out_specs=pl.BlockSpec((window, n_cols, vir_full), lambda s: (0, 0, 0)),
        compiler_params=pltpu.CompilerParams(dimension_semantics=("arbitrary",), vmem_limit_bytes=48 * 1024 * 1024),
    )(vt, g)


def body(occ_irrep, amplitudes, ladder_ints, cycle_ints):
    rows_local, cols_local = amplitudes.shape
    occ_count, vir_part, cycle_cols = cycle_ints.shape
    vir_full = cols_local // vir_part
    vir_local = cycle_cols // occ_count
    pad_rows = -(-rows_local // 16) * 16
    pidx = lax.axis_index(PAIR)
    per_i = occ_count // rows_local
    labels = jnp.concatenate([occ_irrep, jnp.full((pad_rows - rows_local,), -1, occ_irrep.dtype)])
    label_first = lax.dynamic_slice(occ_irrep, (pidx // per_i,), (1,))
    label_second = lax.dynamic_slice(labels, ((pidx % per_i) * rows_local,), (pad_rows,))
    row = lax.broadcasted_iota(jnp.int32, (pad_rows,), 0)
    allowed = (label_second == label_first) & (row < rows_local)
    amp_pad = jnp.where(allowed[:, None], jnp.pad(amplitudes, ((0, pad_rows - rows_local), (0, 0))),
                        jnp.zeros((), amplitudes.dtype))
    g2 = lax.all_gather(amp_pad, PAIR, axis=0, tiled=True)
    n_blocks = g2.shape[0] // pad_rows
    total_rows = n_blocks * rows_local
    window = total_rows // occ_count

    ladder = jnp.dot(g2, ladder_ints, preferred_element_type=jnp.float32)
    ladder = ladder.reshape(n_blocks, pad_rows, -1)[:, :rows_local, :]
    ladder = ladder.reshape(window, occ_count, vir_local * vir_full)

    v4 = cycle_ints.reshape(per_i, rows_local, vir_part, cycle_cols)
    v4 = jnp.pad(v4, ((0, 0), (0, pad_rows - rows_local), (0, 0), (0, 0)))
    vt = jnp.transpose(v4, (2, 3, 0, 1)).reshape(vir_part, cycle_cols, per_i * pad_rows)
    cyc = cycle_matmul(vt, g2, window, vir_full)
    same_irrep = (occ_irrep[:window][:, None] == occ_irrep[None, :]).astype(jnp.float32)
    cyc = cyc.reshape(window, vir_local, occ_count, vir_full)
    cyc = lax.psum_scatter(cyc, "x", scatter_dimension=0, tiled=True)
    rows_here = cyc.shape[0]
    same_here = lax.dynamic_slice_in_dim(same_irrep, lax.axis_index("x") * rows_here, rows_here, axis=0)
    cyc = cyc * same_here[:, None, :, None]
    cycle_term = jnp.transpose(cyc, (0, 3, 1, 2))
    regrouped = lax.all_to_all(cycle_term, PAIR, split_axis=1, concat_axis=2, tiled=True)
    moved = jnp.transpose(regrouped, (0, 3, 1, 2)).reshape(rows_here, occ_count, vir_local * vir_full)
    ladder = lax.psum_scatter(ladder, "x", scatter_dimension=0, tiled=True)
    return ladder + moved


def solution(mesh):
    devs = mesh.devices
    n_pair, n_int = devs.shape
    fine = Mesh(devs.reshape(4, n_pair // 8, 2, n_int), ("z", "y", "core", "x"))
    placed = (P(), P(PAIR, "x"), P("x", PAIR), P(None, "x", PAIR))
    return jax.shard_map(body, mesh=fine, in_specs=placed, out_specs=P("x", None, PAIR), check_vma=False)
```
